768 devices in a mesh: dp: 96 (over x, z, core), zero: 8 (over y).
Axes of the slice: x: 4, y: 8, z: 12, core: 2. Of those that a mesh axis runs over, the one named last changes fastest.
Arguments:
- grad_parts: bfloat16 [96, 3, 704, 1024], P('dp', None, 'zero'), may hold values from -1.5 to 1.5
- momentum: float32 [3, 704, 1024], P(None, 'zero')
- owner_table: int32 [3], replicated, may hold values from 0 to 7, as said below
Outputs:
- new_momentum: float32 [3, 704, 1024], P(None, 'zero')
- update: bfloat16 [3, 704, 1024], P(None, 'zero')
- owner_copy: bfloat16 [8, 704, 1024], P('zero')
The draws below stay inside these ranges and needn't reach their ends.
Inputs may be any that keep to these rules, and one draw needn't show every extreme that they name: `owner_table`: the 3 entries are distinct; the first and the last device along zero always own a matrix.
All inputs are finite; a program needn't handle non-finite values.
Results may differ from the reference program's by a relative error of at most 0.0062.
Values may be sent and summed in bfloat16 or wider, within the bound.
No kernel may reach another device: no remote copies, remote signals or barrier semaphores. Data moves between devices by JAX's collectives and lax.ppermute only.
A program may use at most 32 MiB of HBM per device.

```python
import math
import jax
import jax.numpy as jnp
from jax import lax

D = 1024
HID = 704
MATS = 3
ITERS = 2
N_DP = 96
N_ZERO = 8


def draw_momentum(key, part):
    key_base, key_row, key_col = jax.random.split(key, 3)
    place = jnp.arange(HID, dtype=jnp.float32) / max(HID - 1, 1)
    trend = jnp.exp(math.log(3.0) * place)
    row_scale = jnp.exp(jax.random.uniform(key_row, (HID,), minval=0.0, maxval=math.log(10.0)))
    col_scale = jnp.exp(jax.random.uniform(key_col, (D,), minval=0.0, maxval=math.log(10.0)))
    base = jax.random.normal(key_base, (MATS, HID, D))
    factor = 0.05
    scaled = base * (trend * row_scale)[None, :, None] * col_scale[None, None, :] * factor
    return scaled.astype(jnp.float32)


def distinct_order(key, count):
    scores = jax.random.randint(key, (count,), 0, 1048576, dtype=jnp.int32) * count + jnp.arange(count, dtype=jnp.int32)
    return jnp.argsort(scores, stable=True).astype(jnp.int32)


def draw_owner_table(key, part):
    key_middle = jax.random.fold_in(key, 7101)
    key_order = jax.random.fold_in(key, 7202)
    middle = distinct_order(key_middle, N_ZERO - 2) + 1
    ends = jnp.array([0, N_ZERO - 1], dtype=jnp.int32)
    owners = jnp.concatenate([ends, middle.astype(jnp.int32)])[:MATS]
    order = distinct_order(key_order, MATS)
    return owners[order].astype(jnp.int32)


def levels(stream_key, extent, shards, low, largest):
    loudness = 1.0
    for position, parts in shards:
        draws = jax.random.uniform(jax.random.fold_in(jax.random.fold_in(stream_key, 6), position), (parts,), jnp.float32, low / len(shards), largest / len(shards))
        loudness = loudness * jnp.repeat(jnp.exp(draws), extent[position] // parts).reshape((-1,) + (1,) * (len(extent) - 1 - position))
    return loudness


def normal_values(own_key, shape, scale, reach, cuts=(), held_as=jnp.bfloat16):
    drawn = scale * jax.random.normal(own_key, shape, jnp.float32)
    if cuts:
        drawn = drawn * levels(own_key, shape, cuts, -0.22, 0.18)
    return jnp.clip(drawn, -reach, reach).astype(held_as)


def setup_inputs(seed: int = 0) -> dict:
    key_list = jax.random.split(jax.random.key(seed), 4)
    grad_parts = normal_values(key_list[0], (N_DP, MATS, HID, D), 0.1, 1.5, ((0, 96), (2, 8)))
    momentum = draw_momentum(jax.random.fold_in(key_list[3], 71), 0)
    owner_table = draw_owner_table(jax.random.fold_in(key_list[3], 71), 0)
    return {"grad_parts": grad_parts, "momentum": momentum, "owner_table": owner_table}


COEF_A = 3.4445
COEF_B = -4.775
COEF_C = 2.0315
MOMENTUM_DECAY = 0.95
NORM_EPSILON = 1e-07

def orthogonalize(matrix):
    current = matrix
    iterate = matrix.astype(jnp.float32)
    for step in range(ITERS):
        gram_matrix = jnp.dot(current, current.T, preferred_element_type=jnp.float32).astype(jnp.bfloat16)
        squared = jnp.dot(gram_matrix, gram_matrix, preferred_element_type=jnp.float32)
        poly_term = (COEF_B * gram_matrix.astype(jnp.float32) + COEF_C * squared).astype(jnp.bfloat16)
        iterate = COEF_A * current.astype(jnp.float32) + jnp.dot(poly_term, current, preferred_element_type=jnp.float32)
        if step + 1 < ITERS:
            current = iterate.astype(jnp.bfloat16)
    return (0.2 * math.sqrt(D) * iterate).astype(jnp.bfloat16)

def add_replica(running, replica):
    return (running + replica.astype(jnp.float32), None)

def reference(grad_parts, momentum, owner_table):
    summed, _ = lax.scan(add_replica, jnp.zeros(grad_parts.shape[1:], jnp.float32), grad_parts)
    new_momentum = MOMENTUM_DECAY * momentum + summed
    norms = jnp.sqrt(lax.optimization_barrier(jnp.sum(new_momentum * new_momentum, axis=(1, 2))))
    start_rows = (new_momentum / (norms[:, None, None] + NORM_EPSILON)).astype(jnp.bfloat16)
    update = lax.map(orthogonalize, start_rows)
    onehot = (owner_table[None, :] == jnp.arange(N_ZERO, dtype=jnp.int32)[:, None]).astype(jnp.float32)
    owner_copy = jnp.einsum('oj,jrd->ord', onehot, update.astype(jnp.float32)).astype(jnp.bfloat16)
    return (new_momentum, update, owner_copy)
```

```python
import math

import jax
import jax.numpy as jnp
from jax import lax
from jax.sharding import PartitionSpec as P

D = 1024
ITERS = 2


COEF_A = 3.4445
COEF_B = -4.775
COEF_C = 2.0315
MOMENTUM_DECAY = 0.95
NORM_EPSILON = 1e-07


def orthogonalize(matrix):
    current = matrix
    iterate = matrix.astype(jnp.float32)
    for step in range(ITERS):
        gram_matrix = jnp.dot(current, current.T, preferred_element_type=jnp.float32).astype(
            jnp.bfloat16
        )
        squared = jnp.dot(gram_matrix, gram_matrix, preferred_element_type=jnp.float32)
        poly_term = (COEF_B * gram_matrix.astype(jnp.float32) + COEF_C * squared).astype(
            jnp.bfloat16
        )
        iterate = COEF_A * current.astype(jnp.float32) + jnp.dot(
            poly_term, current, preferred_element_type=jnp.float32
        )
        if step + 1 < ITERS:
            current = iterate.astype(jnp.bfloat16)
    return (0.2 * math.sqrt(D) * iterate).astype(jnp.bfloat16)


def on_device(grad_parts, momentum, owner_table):
    my_index = lax.axis_index("zero")
    n_dp = lax.axis_size("dp")
    local_part = grad_parts[0]
    chunk = local_part.size // n_dp
    pieces = lax.all_to_all(local_part.reshape(n_dp, chunk), "dp", 0, 0, tiled=True)
    summed_chunk = jnp.sum(pieces.astype(jnp.float32), axis=0, keepdims=True)
    dp_index = lax.axis_index("dp")
    momentum_chunk = lax.dynamic_slice_in_dim(momentum.reshape(n_dp, chunk), dp_index, 1, 0)
    new_chunk = MOMENTUM_DECAY * momentum_chunk + summed_chunk
    spread = jnp.broadcast_to(new_chunk, (n_dp, chunk))
    new_momentum = lax.all_to_all(spread, "dp", 0, 0, tiled=True).reshape(momentum.shape)
    partial_value = jnp.sum(new_momentum * new_momentum, axis=(1, 2))
    squares = lax.psum(partial_value, "zero")
    inverse = 1.0 / (jnp.sqrt(squares) + NORM_EPSILON)
    start_rows = (new_momentum * inverse[:, None, None]).astype(jnp.bfloat16)
    mine_mask = (owner_table == my_index).astype(jnp.bfloat16)
    gathered = lax.all_gather(start_rows, "zero", axis=1, tiled=True)
    full_matrix = jnp.einsum(
        "j,jrd->rd", mine_mask, gathered, preferred_element_type=jnp.float32
    ).astype(jnp.bfloat16)
    result = orthogonalize(full_matrix)
    contrib = mine_mask.astype(jnp.float32)[:, None, None] * result.astype(jnp.float32)[None]
    update_rows = lax.psum_scatter(
        contrib.astype(jnp.bfloat16), "zero", scatter_dimension=1, tiled=True
    )
    return (new_momentum, update_rows, result[None])


def solution(mesh):
    placed = (P("dp", None, "zero", None), P(None, "zero", None), P())
    return jax.shard_map(
        on_device,
        mesh=mesh,
        in_specs=placed,
        out_specs=(P(None, "zero", None), P(None, "zero", None), P("zero", None, None)),
        check_vma=False,
    )
```

```python
import math

import jax
import jax.numpy as jnp
from jax import lax
from jax.sharding import PartitionSpec as P

D = 1024
ITERS = 2


COEF_A = 3.4445
COEF_B = -4.775
COEF_C = 2.0315
MOMENTUM_DECAY = 0.95
NORM_EPSILON = 1e-07


def orthogonalize(matrix):
    current = matrix
    iterate = matrix.astype(jnp.float32)
    for step in range(ITERS):
        gram_matrix = jnp.dot(current, current.T, preferred_element_type=jnp.float32).astype(
            jnp.bfloat16
        )
        squared = jnp.dot(gram_matrix, gram_matrix, preferred_element_type=jnp.float32)
        poly_term = (COEF_B * gram_matrix.astype(jnp.float32) + COEF_C * squared).astype(
            jnp.bfloat16
        )
        iterate = COEF_A * current.astype(jnp.float32) + jnp.dot(
            poly_term, current, preferred_element_type=jnp.float32
        )
        if step + 1 < ITERS:
            current = iterate.astype(jnp.bfloat16)
    return (0.2 * math.sqrt(D) * iterate).astype(jnp.bfloat16)


def on_device(grad_parts, momentum, owner_table):
    my_index = lax.axis_index("zero")
    n_dp = lax.axis_size("dp")
    local_part = grad_parts[0]
    chunk = local_part.size // n_dp
    pieces = lax.all_to_all(local_part.reshape(n_dp, chunk), "dp", 0, 0, tiled=True)
    summed_chunk = jnp.sum(pieces.astype(jnp.float32), axis=0, keepdims=True)
    dp_index = lax.axis_index("dp")
    momentum_chunk = lax.dynamic_slice_in_dim(momentum.reshape(n_dp, chunk), dp_index, 1, 0)
    new_chunk = MOMENTUM_DECAY * momentum_chunk + summed_chunk
    spread = jnp.broadcast_to(new_chunk, (n_dp, chunk))
    new_momentum = lax.all_to_all(spread, "dp", 0, 0, tiled=True).reshape(momentum.shape)
    partial_value = jnp.sum(new_momentum * new_momentum, axis=(1, 2))
    squares = lax.psum(partial_value, "zero")
    inverse = 1.0 / (jnp.sqrt(squares) + NORM_EPSILON)
    start_rows = (new_momentum * inverse[:, None, None]).astype(jnp.bfloat16)
    n_zero = lax.axis_size("zero")
    outgoing = jnp.zeros((n_zero,) + start_rows.shape[1:], start_rows.dtype)
    owners = jnp.arange(n_zero, dtype=owner_table.dtype)[:, None, None]
    for j in range(start_rows.shape[0]):
        outgoing = jnp.where(owners == owner_table[j], start_rows[j][None], outgoing)
    incoming = lax.all_to_all(outgoing, "zero", 0, 0, tiled=True)
    full_matrix = incoming.reshape(-1, incoming.shape[-1])
    result = orthogonalize(full_matrix)
    returned = lax.all_to_all(result.reshape(incoming.shape), "zero", 0, 0, tiled=True)
    update_rows = jnp.stack(
        [lax.dynamic_index_in_dim(returned, owner_table[j], 0, keepdims=False)
         for j in range(start_rows.shape[0])]
    )
    return (new_momentum, update_rows, result[None])


def solution(mesh):
    placed = (P("dp", None, "zero", None), P(None, "zero", None), P())
    return jax.shard_map(
        on_device,
        mesh=mesh,
        in_specs=placed,
        out_specs=(P(None, "zero", None), P(None, "zero", None), P("zero", None, None)),
        check_vma=False,
    )
```

```python
import math

import jax
import jax.numpy as jnp
from jax import lax
from jax.sharding import PartitionSpec as P

D = 1024
ITERS = 2


COEF_A = 3.4445
COEF_B = -4.775
COEF_C = 2.0315
MOMENTUM_DECAY = 0.95
NORM_EPSILON = 1e-07


def orthogonalize(matrix):
    current = matrix
    iterate = matrix.astype(jnp.float32)
    for step in range(ITERS):
        gram_matrix = jnp.dot(current, current.T, preferred_element_type=jnp.float32).astype(
            jnp.bfloat16
        )
        squared = jnp.dot(gram_matrix, gram_matrix, preferred_element_type=jnp.float32)
        poly_term = (COEF_B * gram_matrix.astype(jnp.float32) + COEF_C * squared).astype(
            jnp.bfloat16
        )
        iterate = COEF_A * current.astype(jnp.float32) + jnp.dot(
            poly_term, current, preferred_element_type=jnp.float32
        )
        if step + 1 < ITERS:
            current = iterate.astype(jnp.bfloat16)
    return (0.2 * math.sqrt(D) * iterate).astype(jnp.bfloat16)


def on_device(grad_parts, momentum, owner_table):
    my_index = lax.axis_index("zero")
    n_dp = lax.axis_size("dp")
    local_part = grad_parts[0]
    chunk = local_part.size // n_dp
    pieces = lax.all_to_all(local_part.reshape(n_dp, chunk), "dp", 0, 0, tiled=True)
    summed_chunk = jnp.sum(pieces.astype(jnp.float32), axis=0, keepdims=True)
    dp_index = lax.axis_index("dp")
    momentum_chunk = lax.dynamic_slice_in_dim(momentum.reshape(n_dp, chunk), dp_index, 1, 0)
    new_chunk = MOMENTUM_DECAY * momentum_chunk + summed_chunk
    spread = jnp.broadcast_to(new_chunk, (n_dp, chunk))
    new_momentum = lax.all_to_all(spread, "dp", 0, 0, tiled=True).reshape(momentum.shape)
    per_matrix = momentum[0].size
    element = dp_index * chunk + lax.broadcasted_iota(jnp.int32, new_chunk.shape, 1)
    which = element // per_matrix
    squared_chunk = new_chunk * new_chunk
    partial_value = jnp.stack(
        [jnp.sum(jnp.where(which == j, squared_chunk, 0.0)) for j in range(momentum.shape[0])]
    )
    squares = lax.psum(partial_value, ("dp", "zero"))
    inverse = 1.0 / (jnp.sqrt(squares) + NORM_EPSILON)
    start_rows = (new_momentum * inverse[:, None, None]).astype(jnp.bfloat16)
    n_zero = lax.axis_size("zero")
    outgoing = jnp.zeros((n_zero,) + start_rows.shape[1:], start_rows.dtype)
    owners = jnp.arange(n_zero, dtype=owner_table.dtype)[:, None, None]
    for j in range(start_rows.shape[0]):
        outgoing = jnp.where(owners == owner_table[j], start_rows[j][None], outgoing)
    incoming = lax.all_to_all(outgoing, "zero", 0, 0, tiled=True)
    full_matrix = incoming.reshape(-1, incoming.shape[-1])
    result = orthogonalize(full_matrix)
    returned = lax.all_to_all(result.reshape(incoming.shape), "zero", 0, 0, tiled=True)
    update_rows = jnp.stack(
        [lax.dynamic_index_in_dim(returned, owner_table[j], 0, keepdims=False)
         for j in range(start_rows.shape[0])]
    )
    return (new_momentum, update_rows, result[None])


def solution(mesh):
    placed = (P("dp", None, "zero", None), P(None, "zero", None), P())
    return jax.shard_map(
        on_device,
        mesh=mesh,
        in_specs=placed,
        out_specs=(P(None, "zero", None), P(None, "zero", None), P("zero", None, None)),
        check_vma=False,
    )
```

```python
import math

import jax
import jax.numpy as jnp
from jax import lax
from jax.sharding import PartitionSpec as P

D = 1024
ITERS = 2


COEF_A = 3.4445
COEF_B = -4.775
COEF_C = 2.0315
MOMENTUM_DECAY = 0.95
NORM_EPSILON = 1e-07


def orthogonalize(matrix):
    current = matrix
    iterate = matrix.astype(jnp.float32)
    for step in range(ITERS):
        gram_matrix = jnp.dot(current, current.T, preferred_element_type=jnp.float32).astype(
            jnp.bfloat16
        )
        squared = jnp.dot(gram_matrix, gram_matrix, preferred_element_type=jnp.float32)
        poly_term = (COEF_B * gram_matrix.astype(jnp.float32) + COEF_C * squared).astype(
            jnp.bfloat16
        )
        iterate = COEF_A * current.astype(jnp.float32) + jnp.dot(
            poly_term, current, preferred_element_type=jnp.float32
        )
        if step + 1 < ITERS:
            current = iterate.astype(jnp.bfloat16)
    return (0.2 * math.sqrt(D) * iterate).astype(jnp.bfloat16)


def on_device(grad_parts, momentum, owner_table):
    my_index = lax.axis_index("zero")
    n_dp = lax.axis_size("dp")
    local_part = grad_parts[0]
    chunk = local_part.size // n_dp
    pieces = lax.all_to_all(local_part.reshape(n_dp, chunk), "dp", 0, 0, tiled=True)
    summed_chunk = jnp.sum(pieces.astype(jnp.float32), axis=0, keepdims=True)
    dp_index = lax.axis_index("dp")
    momentum_chunk = lax.dynamic_slice_in_dim(momentum.reshape(n_dp, chunk), dp_index, 1, 0)
    new_chunk = MOMENTUM_DECAY * momentum_chunk + summed_chunk
    spread = jnp.broadcast_to(new_chunk, (n_dp, chunk))
    new_momentum = lax.all_to_all(spread, "dp", 0, 0, tiled=True).reshape(momentum.shape)
    partial_value = jnp.sum(new_momentum * new_momentum, axis=(1, 2))
    squares = lax.psum(partial_value, "zero")
    inverse = 1.0 / (jnp.sqrt(squares) + NORM_EPSILON)
    start_rows = (new_momentum * inverse[:, None, None]).astype(jnp.bfloat16)
    n_zero = lax.axis_size("zero")
    core = dp_index % 2
    siblings = [(d, d ^ 1) for d in range(n_dp)]
    width = start_rows.shape[-1] // 2

    def own_half(blocks):
        return lax.dynamic_slice_in_dim(blocks, core * width, width, axis=2)

    def both_halves(mine):
        other = lax.ppermute(mine, "dp", siblings)
        return jnp.where(core == 0, jnp.concatenate([mine, other], axis=2),
                         jnp.concatenate([other, mine], axis=2))

    outgoing = jnp.zeros((n_zero,) + start_rows.shape[1:], start_rows.dtype)
    owners = jnp.arange(n_zero, dtype=owner_table.dtype)[:, None, None]
    for j in range(start_rows.shape[0]):
        outgoing = jnp.where(owners == owner_table[j], start_rows[j][None], outgoing)
    incoming = both_halves(lax.all_to_all(own_half(outgoing), "zero", 0, 0, tiled=True))
    full_matrix = incoming.reshape(-1, incoming.shape[-1])
    result = orthogonalize(full_matrix)
    back = lax.all_to_all(own_half(result.reshape(incoming.shape)), "zero", 0, 0, tiled=True)
    returned = both_halves(back)
    update_rows = jnp.stack(
        [lax.dynamic_index_in_dim(returned, owner_table[j], 0, keepdims=False)
         for j in range(start_rows.shape[0])]
    )
    return (new_momentum, update_rows, result[None])


def solution(mesh):
    placed = (P("dp", None, "zero", None), P(None, "zero", None), P())
    return jax.shard_map(
        on_device,
        mesh=mesh,
        in_specs=placed,
        out_specs=(P(None, "zero", None), P(None, "zero", None), P("zero", None, None)),
        check_vma=False,
    )
```

```python
import math

import jax
import jax.numpy as jnp
from jax import lax
from jax.sharding import Mesh, PartitionSpec as P

D = 1024
ITERS = 2


COEF_A = 3.4445
COEF_B = -4.775
COEF_C = 2.0315
MOMENTUM_DECAY = 0.95
NORM_EPSILON = 1e-07
DP = ("chip", "core")


def orthogonalize(matrix):
    current = matrix
    iterate = matrix.astype(jnp.float32)
    for step in range(ITERS):
        gram_matrix = jnp.dot(current, current.T, preferred_element_type=jnp.float32).astype(
            jnp.bfloat16
        )
        squared = jnp.dot(gram_matrix, gram_matrix, preferred_element_type=jnp.float32)
        poly_term = (COEF_B * gram_matrix.astype(jnp.float32) + COEF_C * squared).astype(
            jnp.bfloat16
        )
        iterate = COEF_A * current.astype(jnp.float32) + jnp.dot(
            poly_term, current, preferred_element_type=jnp.float32
        )
        if step + 1 < ITERS:
            current = iterate.astype(jnp.bfloat16)
    return (0.2 * math.sqrt(D) * iterate).astype(jnp.bfloat16)


def on_device(grad_parts, momentum, owner_table):
    my_index = lax.axis_index("zero")
    n_chip = lax.axis_size("chip")
    n_dp = n_chip * lax.axis_size("core")
    core = lax.axis_index("core")
    local_part = grad_parts[0]
    chunk = local_part.size // n_dp
    pieces = lax.all_to_all(local_part.reshape(n_dp, chunk), DP, 0, 0, tiled=True)
    summed_chunk = jnp.sum(pieces.astype(jnp.float32), axis=0, keepdims=True)
    dp_index = lax.axis_index("chip") * 2 + core
    momentum_chunk = lax.dynamic_slice_in_dim(momentum.reshape(n_dp, chunk), dp_index, 1, 0)
    new_chunk = MOMENTUM_DECAY * momentum_chunk + summed_chunk
    spread = jnp.broadcast_to(new_chunk, (n_chip, chunk))
    mine = lax.all_to_all(spread, "chip", 0, 0, tiled=True)
    other = lax.ppermute(mine, "core", [(0, 1), (1, 0)])
    ordered = jnp.where(core == 0, jnp.stack([mine, other], axis=1), jnp.stack([other, mine], axis=1))
    new_momentum = ordered.reshape(momentum.shape)
    partial_value = jnp.sum(new_momentum * new_momentum, axis=(1, 2))
    squares = lax.psum(partial_value, "zero")
    inverse = 1.0 / (jnp.sqrt(squares) + NORM_EPSILON)
    start_rows = (new_momentum * inverse[:, None, None]).astype(jnp.bfloat16)
    n_zero = lax.axis_size("zero")
    width = start_rows.shape[-1] // 2

    def own_half(blocks):
        return lax.dynamic_slice_in_dim(blocks, core * width, width, axis=2)

    def both_halves(mine):
        other = lax.ppermute(mine, "core", [(0, 1), (1, 0)])
        return jnp.where(core == 0, jnp.concatenate([mine, other], axis=2),
                         jnp.concatenate([other, mine], axis=2))

    outgoing = jnp.zeros((n_zero,) + start_rows.shape[1:], start_rows.dtype)
    owners = jnp.arange(n_zero, dtype=owner_table.dtype)[:, None, None]
    for j in range(start_rows.shape[0]):
        outgoing = jnp.where(owners == owner_table[j], start_rows[j][None], outgoing)
    incoming = both_halves(lax.all_to_all(own_half(outgoing), "zero", 0, 0, tiled=True))
    full_matrix = incoming.reshape(-1, incoming.shape[-1])
    result = orthogonalize(full_matrix)
    back = lax.all_to_all(own_half(result.reshape(incoming.shape)), "zero", 0, 0, tiled=True)
    returned = both_halves(back)
    update_rows = jnp.stack(
        [lax.dynamic_index_in_dim(returned, owner_table[j], 0, keepdims=False)
         for j in range(start_rows.shape[0])]
    )
    return (new_momentum, update_rows, result[None])


def solution(mesh):
    n_dp, n_zero = mesh.devices.shape
    split = Mesh(mesh.devices.reshape(n_dp // 2, 2, n_zero), ("chip", "core", "zero"))
    placed = (P(DP, None, "zero", None), P(None, "zero", None), P())
    return jax.shard_map(
        on_device,
        mesh=split,
        in_specs=placed,
        out_specs=(P(None, "zero", None), P(None, "zero", None), P("zero", None, None)),
        check_vma=False,
    )
```

```python
import math

import jax
import jax.numpy as jnp
from jax import lax
from jax.sharding import Mesh, PartitionSpec as P

D = 1024
ITERS = 2


COEF_A = 3.4445
COEF_B = -4.775
COEF_C = 2.0315
MOMENTUM_DECAY = 0.95
NORM_EPSILON = 1e-07
DP = ("chip", "core")


def orthogonalize(matrix):
    current = matrix
    iterate = matrix.astype(jnp.float32)
    for step in range(ITERS):
        gram_matrix = jnp.dot(current, current.T, preferred_element_type=jnp.float32).astype(
            jnp.bfloat16
        )
        squared = jnp.dot(gram_matrix, gram_matrix, preferred_element_type=jnp.float32)
        poly_term = (COEF_B * gram_matrix.astype(jnp.float32) + COEF_C * squared).astype(
            jnp.bfloat16
        )
        iterate = COEF_A * current.astype(jnp.float32) + jnp.dot(
            poly_term, current, preferred_element_type=jnp.float32
        )
        if step + 1 < ITERS:
            current = iterate.astype(jnp.bfloat16)
    return (0.2 * math.sqrt(D) * iterate).astype(jnp.bfloat16)


def on_device(grad_parts, momentum, owner_table):
    my_index = lax.axis_index("zero")
    n_chip = lax.axis_size("chip")
    n_dp = n_chip * lax.axis_size("core")
    core = lax.axis_index("core")
    local_part = grad_parts[0]
    chunk = local_part.size // n_dp
    by_core = local_part.reshape(n_chip, 2, chunk)
    kept = lax.dynamic_index_in_dim(by_core, core, axis=1, keepdims=False)
    given = lax.dynamic_index_in_dim(by_core, 1 - core, axis=1, keepdims=False)
    taken = lax.ppermute(given, "core", [(0, 1), (1, 0)])
    pieces = lax.all_to_all(jnp.stack([kept, taken], axis=1), "chip", 0, 0, tiled=True)
    summed_chunk = jnp.sum(pieces.astype(jnp.float32), axis=(0, 1))[None]
    dp_index = lax.axis_index("chip") * 2 + core
    momentum_chunk = lax.dynamic_slice_in_dim(momentum.reshape(n_dp, chunk), dp_index, 1, 0)
    new_chunk = MOMENTUM_DECAY * momentum_chunk + summed_chunk
    spread = jnp.broadcast_to(new_chunk, (n_chip, chunk))
    mine = lax.all_to_all(spread, "chip", 0, 0, tiled=True)
    other = lax.ppermute(mine, "core", [(0, 1), (1, 0)])
    ordered = jnp.where(core == 0, jnp.stack([mine, other], axis=1), jnp.stack([other, mine], axis=1))
    new_momentum = ordered.reshape(momentum.shape)
    partial_value = jnp.sum(new_momentum * new_momentum, axis=(1, 2))
    squares = lax.psum(partial_value, "zero")
    inverse = 1.0 / (jnp.sqrt(squares) + NORM_EPSILON)
    start_rows = (new_momentum * inverse[:, None, None]).astype(jnp.bfloat16)
    n_zero = lax.axis_size("zero")
    width = start_rows.shape[-1] // 2

    def own_half(blocks):
        return lax.dynamic_slice_in_dim(blocks, core * width, width, axis=2)

    def both_halves(mine):
        other = lax.ppermute(mine, "core", [(0, 1), (1, 0)])
        return jnp.where(core == 0, jnp.concatenate([mine, other], axis=2),
                         jnp.concatenate([other, mine], axis=2))

    outgoing = jnp.zeros((n_zero,) + start_rows.shape[1:], start_rows.dtype)
    owners = jnp.arange(n_zero, dtype=owner_table.dtype)[:, None, None]
    for j in range(start_rows.shape[0]):
        outgoing = jnp.where(owners == owner_table[j], start_rows[j][None], outgoing)
    incoming = both_halves(lax.all_to_all(own_half(outgoing), "zero", 0, 0, tiled=True))
    full_matrix = incoming.reshape(-1, incoming.shape[-1])
    result = orthogonalize(full_matrix)
    back = lax.all_to_all(own_half(result.reshape(incoming.shape)), "zero", 0, 0, tiled=True)
    returned = both_halves(back)
    update_rows = jnp.stack(
        [lax.dynamic_index_in_dim(returned, owner_table[j], 0, keepdims=False)
         for j in range(start_rows.shape[0])]
    )
    return (new_momentum, update_rows, result[None])


def solution(mesh):
    n_dp, n_zero = mesh.devices.shape
    split = Mesh(mesh.devices.reshape(n_dp // 2, 2, n_zero), ("chip", "core", "zero"))
    placed = (P(DP, None, "zero", None), P(None, "zero", None), P())
    return jax.shard_map(
        on_device,
        mesh=split,
        in_specs=placed,
        out_specs=(P(None, "zero", None), P(None, "zero", None), P("zero", None, None)),
        check_vma=False,
    )
```

```python
import math

import jax
import jax.numpy as jnp
from jax import lax
from jax.sharding import Mesh, PartitionSpec as P

D = 1024
ITERS = 2


COEF_A = 3.4445
COEF_B = -4.775
COEF_C = 2.0315
MOMENTUM_DECAY = 0.95
NORM_EPSILON = 1e-07
DP = ("chip", "core")


def orthogonalize(matrix):
    current = matrix
    iterate = matrix.astype(jnp.float32)
    for step in range(ITERS):
        gram_matrix = jnp.dot(current, current.T, preferred_element_type=jnp.float32).astype(
            jnp.bfloat16
        )
        squared = jnp.dot(gram_matrix, gram_matrix, preferred_element_type=jnp.float32)
        poly_term = (COEF_B * gram_matrix.astype(jnp.float32) + COEF_C * squared).astype(
            jnp.bfloat16
        )
        iterate = COEF_A * current.astype(jnp.float32) + jnp.dot(
            poly_term, current, preferred_element_type=jnp.float32
        )
        if step + 1 < ITERS:
            current = iterate.astype(jnp.bfloat16)
    return (0.2 * math.sqrt(D) * iterate).astype(jnp.bfloat16)


def on_device(grad_parts, momentum, owner_table):
    my_index = lax.axis_index("zero")
    n_chip = lax.axis_size("chip")
    n_dp = n_chip * lax.axis_size("core")
    core = lax.axis_index("core")
    local_part = grad_parts[0]
    chunk = local_part.size // n_dp
    pieces = lax.all_to_all(local_part.reshape(n_dp, chunk), DP, 0, 0, tiled=True)
    summed_chunk = jnp.sum(pieces.astype(jnp.float32), axis=0, keepdims=True)
    dp_index = lax.axis_index("chip") * 2 + core
    momentum_chunk = lax.dynamic_slice_in_dim(momentum.reshape(n_dp, chunk), dp_index, 1, 0)
    new_chunk = MOMENTUM_DECAY * momentum_chunk + summed_chunk
    spread = jnp.broadcast_to(new_chunk, (n_chip, chunk))
    mine = lax.all_to_all(spread, "chip", 0, 0, tiled=True)
    other = lax.ppermute(mine, "core", [(0, 1), (1, 0)])
    ordered = jnp.where(core == 0, jnp.stack([mine, other], axis=1), jnp.stack([other, mine], axis=1))
    new_momentum = ordered.reshape(momentum.shape)
    n_zero = lax.axis_size("zero")
    width = new_momentum.shape[-1] // 2

    def own_half(blocks):
        return lax.dynamic_slice_in_dim(blocks, core * width, width, axis=2)

    def both_halves(mine):
        other = lax.ppermute(mine, "core", [(0, 1), (1, 0)])
        return jnp.where(core == 0, jnp.concatenate([mine, other], axis=2),
                         jnp.concatenate([other, mine], axis=2))

    outgoing = jnp.zeros((n_zero,) + new_momentum.shape[1:], new_momentum.dtype)
    owners = jnp.arange(n_zero, dtype=owner_table.dtype)[:, None, None]
    for j in range(new_momentum.shape[0]):
        outgoing = jnp.where(owners == owner_table[j], new_momentum[j][None], outgoing)
    incoming = both_halves(lax.all_to_all(own_half(outgoing), "zero", 0, 0, tiled=True))
    owned = incoming.reshape(-1, incoming.shape[-1])
    norm = jnp.sqrt(jnp.sum(owned * owned))
    full_matrix = (owned / (norm + NORM_EPSILON)).astype(jnp.bfloat16)
    result = orthogonalize(full_matrix)
    back = lax.all_to_all(own_half(result.reshape(incoming.shape)), "zero", 0, 0, tiled=True)
    returned = both_halves(back)
    update_rows = jnp.stack(
        [lax.dynamic_index_in_dim(returned, owner_table[j], 0, keepdims=False)
         for j in range(new_momentum.shape[0])]
    )
    return (new_momentum, update_rows, result[None])


def solution(mesh):
    n_dp, n_zero = mesh.devices.shape
    split = Mesh(mesh.devices.reshape(n_dp // 2, 2, n_zero), ("chip", "core", "zero"))
    placed = (P(DP, None, "zero", None), P(None, "zero", None), P())
    return jax.shard_map(
        on_device,
        mesh=split,
        in_specs=placed,
        out_specs=(P(None, "zero", None), P(None, "zero", None), P("zero", None, None)),
        check_vma=False,
    )
```

```python
import math

import jax
import jax.numpy as jnp
from jax import lax
from jax.sharding import Mesh, PartitionSpec as P

D = 1024
ITERS = 2


COEF_A = 3.4445
COEF_B = -4.775
COEF_C = 2.0315
MOMENTUM_DECAY = 0.95
NORM_EPSILON = 1e-07
DP = ("chip", "core")


def orthogonalize(matrix):
    current = matrix
    iterate = matrix.astype(jnp.float32)
    for step in range(ITERS):
        gram_matrix = jnp.dot(current, current.T, preferred_element_type=jnp.float32).astype(
            jnp.bfloat16
        )
        squared = jnp.dot(gram_matrix, gram_matrix, preferred_element_type=jnp.float32)
        poly_term = (COEF_B * gram_matrix.astype(jnp.float32) + COEF_C * squared).astype(
            jnp.bfloat16
        )
        iterate = COEF_A * current.astype(jnp.float32) + jnp.dot(
            poly_term, current, preferred_element_type=jnp.float32
        )
        if step + 1 < ITERS:
            current = iterate.astype(jnp.bfloat16)
    return (0.2 * math.sqrt(D) * iterate).astype(jnp.bfloat16)


def on_device(grad_parts, momentum, owner_table):
    my_index = lax.axis_index("zero")
    n_chip = lax.axis_size("chip")
    n_dp = n_chip * lax.axis_size("core")
    core = lax.axis_index("core")
    local_part = grad_parts[0]
    chunk = local_part.size // n_dp
    pieces = lax.all_to_all(local_part.reshape(n_dp, chunk), DP, 0, 0, tiled=True)
    summed_chunk = jnp.sum(pieces.astype(jnp.float32), axis=0, keepdims=True)
    dp_index = lax.axis_index("chip") * 2 + core
    momentum_chunk = lax.dynamic_slice_in_dim(momentum.reshape(n_dp, chunk), dp_index, 1, 0)
    new_chunk = MOMENTUM_DECAY * momentum_chunk + summed_chunk
    spread = jnp.broadcast_to(new_chunk, (n_chip, chunk))
    mine = lax.all_to_all(spread, "chip", 0, 0, tiled=True)
    other = lax.ppermute(mine, "core", [(0, 1), (1, 0)])
    ordered = jnp.where(core == 0, jnp.stack([mine, other], axis=1), jnp.stack([other, mine], axis=1))
    new_momentum = ordered.reshape(momentum.shape)
    partial_value = jnp.sum(new_momentum * new_momentum, axis=(1, 2))
    n_zero = lax.axis_size("zero")
    spread_sums = jnp.broadcast_to(partial_value[None], (n_zero,) + partial_value.shape)
    squares = jnp.sum(lax.all_to_all(spread_sums, "zero", 0, 0, tiled=True), axis=0)
    inverse = 1.0 / (jnp.sqrt(squares) + NORM_EPSILON)
    start_rows = (new_momentum * inverse[:, None, None]).astype(jnp.bfloat16)
    n_zero = lax.axis_size("zero")
    width = start_rows.shape[-1] // 2

    def own_half(blocks):
        return lax.dynamic_slice_in_dim(blocks, core * width, width, axis=2)

    def both_halves(mine):
        other = lax.ppermute(mine, "core", [(0, 1), (1, 0)])
        return jnp.where(core == 0, jnp.concatenate([mine, other], axis=2),
                         jnp.concatenate([other, mine], axis=2))

    outgoing = jnp.zeros((n_zero,) + start_rows.shape[1:], start_rows.dtype)
    owners = jnp.arange(n_zero, dtype=owner_table.dtype)[:, None, None]
    for j in range(start_rows.shape[0]):
        outgoing = jnp.where(owners == owner_table[j], start_rows[j][None], outgoing)
    incoming = both_halves(lax.all_to_all(own_half(outgoing), "zero", 0, 0, tiled=True))
    full_matrix = incoming.reshape(-1, incoming.shape[-1])
    result = orthogonalize(full_matrix)
    back = lax.all_to_all(own_half(result.reshape(incoming.shape)), "zero", 0, 0, tiled=True)
    returned = both_halves(back)
    update_rows = jnp.stack(
        [lax.dynamic_index_in_dim(returned, owner_table[j], 0, keepdims=False)
         for j in range(start_rows.shape[0])]
    )
    return (new_momentum, update_rows, result[None])


def solution(mesh):
    n_dp, n_zero = mesh.devices.shape
    split = Mesh(mesh.devices.reshape(n_dp // 2, 2, n_zero), ("chip", "core", "zero"))
    placed = (P(DP, None, "zero", None), P(None, "zero", None), P())
    return jax.shard_map(
        on_device,
        mesh=split,
        in_specs=placed,
        out_specs=(P(None, "zero", None), P(None, "zero", None), P("zero", None, None)),
        check_vma=False,
    )
```

```python
import math

import jax
import jax.numpy as jnp
from jax import lax
from jax.sharding import Mesh, PartitionSpec as P

D = 1024
ITERS = 2


COEF_A = 3.4445
COEF_B = -4.775
COEF_C = 2.0315
MOMENTUM_DECAY = 0.95
NORM_EPSILON = 1e-07
DP = ("chip", "core")


def orthogonalize(matrix):
    current = matrix
    iterate = matrix.astype(jnp.float32)
    for step in range(ITERS):
        gram_matrix = jnp.dot(current, current.T, preferred_element_type=jnp.float32).astype(
            jnp.bfloat16
        )
        squared = jnp.dot(gram_matrix, gram_matrix, preferred_element_type=jnp.float32)
        poly_term = (COEF_B * gram_matrix.astype(jnp.float32) + COEF_C * squared).astype(
            jnp.bfloat16
        )
        iterate = COEF_A * current.astype(jnp.float32) + jnp.dot(
            poly_term, current, preferred_element_type=jnp.float32
        )
        if step + 1 < ITERS:
            current = iterate.astype(jnp.bfloat16)
    return (0.2 * math.sqrt(D) * iterate).astype(jnp.bfloat16)


def on_device(grad_parts, momentum, owner_table):
    my_index = lax.axis_index("zero")
    n_chip = lax.axis_size("chip")
    n_dp = n_chip * lax.axis_size("core")
    core = lax.axis_index("core")
    local_part = grad_parts[0]
    chunk = local_part.size // n_dp
    pieces = lax.all_to_all(local_part.reshape(n_dp, chunk), DP, 0, 0, tiled=True)
    summed_chunk = jnp.sum(pieces.astype(jnp.float32), axis=0, keepdims=True)
    dp_index = lax.axis_index("chip") * 2 + core
    momentum_chunk = lax.dynamic_slice_in_dim(momentum.reshape(n_dp, chunk), dp_index, 1, 0)
    new_chunk = MOMENTUM_DECAY * momentum_chunk + summed_chunk
    spread = jnp.broadcast_to(new_chunk, (n_chip, chunk))
    mine = lax.all_to_all(spread, "chip", 0, 0, tiled=True)
    other = lax.ppermute(mine, "core", [(0, 1), (1, 0)])
    ordered = jnp.where(core == 0, jnp.stack([mine, other], axis=1), jnp.stack([other, mine], axis=1))
    new_momentum = ordered.reshape(momentum.shape)
    partial_value = jnp.sum(new_momentum * new_momentum, axis=(1, 2))
    n_zero = lax.axis_size("zero")
    spread_sums = jnp.broadcast_to(partial_value[None], (n_zero,) + partial_value.shape)
    squares = jnp.sum(lax.all_to_all(spread_sums, "zero", 0, 0, tiled=True), axis=0)
    inverse = 1.0 / (jnp.sqrt(squares) + NORM_EPSILON)
    start_rows = (new_momentum * inverse[:, None, None]).astype(jnp.bfloat16)
    n_zero = lax.axis_size("zero")
    quarter = core * 2 + lax.axis_index("chip") % 2
    width = start_rows.shape[-1] // 4
    neighbours = [(k, k ^ 1) for k in range(n_chip)]

    def own_half(blocks):
        return lax.dynamic_slice_in_dim(blocks, quarter * width, width, axis=2)

    def both_halves(mine):
        pair_bit = lax.axis_index("chip") % 2
        across = lax.ppermute(mine, "chip", neighbours)
        mine = jnp.where(pair_bit == 0, jnp.concatenate([mine, across], axis=2),
                         jnp.concatenate([across, mine], axis=2))
        other = lax.ppermute(mine, "core", [(0, 1), (1, 0)])
        return jnp.where(core == 0, jnp.concatenate([mine, other], axis=2),
                         jnp.concatenate([other, mine], axis=2))

    outgoing = jnp.zeros((n_zero,) + start_rows.shape[1:], start_rows.dtype)
    owners = jnp.arange(n_zero, dtype=owner_table.dtype)[:, None, None]
    for j in range(start_rows.shape[0]):
        outgoing = jnp.where(owners == owner_table[j], start_rows[j][None], outgoing)
    incoming = both_halves(lax.all_to_all(own_half(outgoing), "zero", 0, 0, tiled=True))
    full_matrix = incoming.reshape(-1, incoming.shape[-1])
    result = orthogonalize(full_matrix)
    back = lax.all_to_all(own_half(result.reshape(incoming.shape)), "zero", 0, 0, tiled=True)
    returned = both_halves(back)
    update_rows = jnp.stack(
        [lax.dynamic_index_in_dim(returned, owner_table[j], 0, keepdims=False)
         for j in range(start_rows.shape[0])]
    )
    return (new_momentum, update_rows, result[None])


def solution(mesh):
    n_dp, n_zero = mesh.devices.shape
    split = Mesh(mesh.devices.reshape(n_dp // 2, 2, n_zero), ("chip", "core", "zero"))
    placed = (P(DP, None, "zero", None), P(None, "zero", None), P())
    return jax.shard_map(
        on_device,
        mesh=split,
        in_specs=placed,
        out_specs=(P(None, "zero", None), P(None, "zero", None), P("zero", None, None)),
        check_vma=False,
    )
```

```python
import math

import jax
import jax.numpy as jnp
from jax import lax
from jax.sharding import Mesh, PartitionSpec as P

D = 1024
ITERS = 2


COEF_A = 3.4445
COEF_B = -4.775
COEF_C = 2.0315
MOMENTUM_DECAY = 0.95
NORM_EPSILON = 1e-07
DP = ("chip", "core")


def orthogonalize(matrix):
    current = matrix
    iterate = matrix.astype(jnp.float32)
    for step in range(ITERS):
        gram_matrix = jnp.dot(current, current.T, preferred_element_type=jnp.float32).astype(
            jnp.bfloat16
        )
        squared = jnp.dot(gram_matrix, gram_matrix, preferred_element_type=jnp.float32)
        poly_term = (COEF_B * gram_matrix.astype(jnp.float32) + COEF_C * squared).astype(
            jnp.bfloat16
        )
        iterate = COEF_A * current.astype(jnp.float32) + jnp.dot(
            poly_term, current, preferred_element_type=jnp.float32
        )
        if step + 1 < ITERS:
            current = iterate.astype(jnp.bfloat16)
    return (0.2 * math.sqrt(D) * iterate).astype(jnp.bfloat16)


def on_device(grad_parts, momentum, owner_table):
    my_index = lax.axis_index("zero")
    n_chip = lax.axis_size("chip")
    n_dp = n_chip * lax.axis_size("core")
    core = lax.axis_index("core")
    local_part = grad_parts[0]
    chunk = local_part.size // n_dp
    pieces = lax.all_to_all(local_part.reshape(n_dp, chunk), DP, 0, 0, tiled=True)
    summed_chunk = jnp.sum(pieces.astype(jnp.float32), axis=0, keepdims=True)
    dp_index = lax.axis_index("chip") * 2 + core
    momentum_chunk = lax.dynamic_slice_in_dim(momentum.reshape(n_dp, chunk), dp_index, 1, 0)
    new_chunk = MOMENTUM_DECAY * momentum_chunk + summed_chunk
    spread = jnp.broadcast_to(new_chunk, (n_chip, chunk))
    mine = lax.all_to_all(spread, "chip", 0, 0, tiled=True)
    other = lax.ppermute(mine, "core", [(0, 1), (1, 0)])
    ordered = jnp.where(core == 0, jnp.stack([mine, other], axis=1), jnp.stack([other, mine], axis=1))
    new_momentum = ordered.reshape(momentum.shape)
    partial_value = jnp.sum(new_momentum * new_momentum, axis=(1, 2))
    n_zero = lax.axis_size("zero")
    spread_sums = jnp.broadcast_to(partial_value[None], (n_zero,) + partial_value.shape)
    squares = jnp.sum(lax.all_to_all(spread_sums, "zero", 0, 0, tiled=True), axis=0)
    inverse = 1.0 / (jnp.sqrt(squares) + NORM_EPSILON)
    start_rows = (new_momentum * inverse[:, None, None]).astype(jnp.bfloat16)
    n_zero = lax.axis_size("zero")
    width = start_rows.shape[-1] // 2

    def own_half(blocks):
        return lax.dynamic_slice_in_dim(blocks, core * width, width, axis=2)

    def both_halves(mine):
        other = lax.ppermute(mine, "core", [(0, 1), (1, 0)])
        return jnp.where(core == 0, jnp.concatenate([mine, other], axis=2),
                         jnp.concatenate([other, mine], axis=2))

    half_rows = own_half(start_rows)
    outgoing = jnp.zeros((n_zero,) + half_rows.shape[1:], half_rows.dtype)
    owners = jnp.arange(n_zero, dtype=owner_table.dtype)[:, None, None]
    for j in range(half_rows.shape[0]):
        outgoing = jnp.where(owners == owner_table[j], half_rows[j][None], outgoing)
    incoming = both_halves(lax.all_to_all(outgoing, "zero", 0, 0, tiled=True))
    full_matrix = incoming.reshape(-1, incoming.shape[-1])
    result = orthogonalize(full_matrix)
    back = lax.all_to_all(own_half(result.reshape(incoming.shape)), "zero", 0, 0, tiled=True)
    returned = both_halves(back)
    update_rows = jnp.stack(
        [lax.dynamic_index_in_dim(returned, owner_table[j], 0, keepdims=False)
         for j in range(start_rows.shape[0])]
    )
    return (new_momentum, update_rows, result[None])


def solution(mesh):
    n_dp, n_zero = mesh.devices.shape
    split = Mesh(mesh.devices.reshape(n_dp // 2, 2, n_zero), ("chip", "core", "zero"))
    placed = (P(DP, None, "zero", None), P(None, "zero", None), P())
    return jax.shard_map(
        on_device,
        mesh=split,
        in_specs=placed,
        out_specs=(P(None, "zero", None), P(None, "zero", None), P("zero", None, None)),
        check_vma=False,
    )
```
